128 devices in a mesh: row: 8 (over z, core), col: 16 (over x, y).
Axes of the slice: x: 4, y: 4, z: 4, core: 2. Of those that a mesh axis runs over, the one named last changes fastest.
Arguments:
- snapshots: float32 [512, 196608], P(('row', 'col')), may hold values from -6 to 6
- panels: float32 [8, 6, 32768, 256], P(None, None, ('row', 'col')), may hold values from -0.1875 to 0.1875
- diag_inverse: float32 [8, 256, 256], replicated, may hold values from -0.6 to 1.5, as said below
Outputs:
- whitened: float32 [6, 32768, 512], P(None, ('row', 'col'))
The draws below stay inside these ranges and needn't reach their ends.
Inputs may be any that keep to these rules, and one draw needn't show every extreme that they name: Each block of diag_inverse is lower triangular with a diagonal of 0.5 to 1.5.
All inputs are finite; a program needn't handle non-finite values.
Results may differ from the reference program's by a relative error of at most 0.0001.
Values sent between devices are 32-bit elements; how exact they have to be, the bound alone decides.
No kernel may reach another device: no remote copies, remote signals or barrier semaphores. Data moves between devices by JAX's collectives and lax.ppermute only.
A program may use at most 128 MiB of HBM per device.

```python
import math
import jax
import jax.numpy as jnp
from jax import lax

NB = 256
STEPS = 8
BLK_DEV = 6
M = 196608
S = 512
DEVICES = 128


def draw_diag_inverse(key, part):
    first_key, second_key = jax.random.split(jax.random.fold_in(key, 17))
    below = jnp.clip(jax.random.normal(first_key, (STEPS, NB, NB), jnp.float32), -4.0, 4.0) * (0.6 / math.sqrt(NB))
    diagonal = jnp.exp(jax.random.uniform(second_key, (STEPS, NB), jnp.float32, math.log(0.5), math.log(1.5)))
    row_index = lax.broadcasted_iota(jnp.int32, (STEPS, NB, NB), 1)
    col_index = lax.broadcasted_iota(jnp.int32, (STEPS, NB, NB), 2)
    return jnp.where(row_index > col_index, below, jnp.where(row_index == col_index, diagonal[:, :, None], 0.0))


def steps_of(rng, shape, cuts, least, top_value):
    def one(dim, blocks):
        heights = jax.random.uniform(jax.random.fold_in(jax.random.fold_in(rng, 6), dim), (blocks,), jnp.float32, least / len(cuts), top_value / len(cuts))
        return jnp.repeat(jnp.exp(heights), shape[dim] // blocks).reshape((-1,) + (1,) * (len(shape) - dim - 1))

    gain = one(*cuts[0])
    for cut in cuts[1:]:
        gain = gain * one(*cut)
    return gain


def normal_values(own_key, extent, spread, limit, cuts=(), kind=jnp.bfloat16):
    array = jax.random.normal(own_key, extent, jnp.float32) * spread
    if len(cuts) > 0:
        array = steps_of(own_key, extent, cuts, -0.22, 0.18) * array
    return jnp.clip(array, min=-limit, max=limit).astype(kind)


def setup_inputs(seed: int = 0) -> dict:
    keys = jax.random.split(jax.random.key(seed), 4)
    snapshots = normal_values(keys[0], (S, M), 1.0, 6.0, ((0, 128),), jnp.float32)
    panels = normal_values(keys[1], (STEPS, BLK_DEV, DEVICES * NB, NB), (4 * NB) ** -0.5, 0.1875, ((2, 128),), jnp.float32)
    diag_inverse = draw_diag_inverse(jax.random.fold_in(keys[3], 71), 0)
    return {"snapshots": snapshots, "panels": panels, "diag_inverse": diag_inverse}


def reference(snapshots, panels, diag_inverse):
    remaining = jnp.transpose(snapshots)
    columns = panels.reshape(panels.shape[0], -1, panels.shape[3])
    row_index = lax.broadcasted_iota(jnp.int32, (remaining.shape[0], 1), 0)
    for section in range(STEPS):
        offset = section * NB
        leading = remaining[offset:offset + NB]
        solved = jnp.dot(diag_inverse[section], leading, precision=lax.Precision.HIGHEST, preferred_element_type=jnp.float32)
        product = jnp.dot(columns[section], solved, precision=lax.Precision.HIGHEST, preferred_element_type=jnp.float32)
        remaining = jnp.where(row_index >= offset + NB, remaining - product, remaining)
        remaining = remaining.at[offset:offset + NB].set(solved)
    return remaining.reshape(BLK_DEV, -1, remaining.shape[1])
```

```python
import jax
import jax.numpy as jnp
from jax import lax
from jax.sharding import PartitionSpec as P

AXES = ("row", "col")
HI = lax.Precision.HIGHEST


def mm(a, b):
    return jnp.dot(a, b, precision=HI, preferred_element_type=jnp.float32)


def tree_round(buf, root, level, devices):
    step = 2**level
    pairs = [((root + r) % devices, (root + r + step) % devices) for r in range(step)]
    return lax.ppermute(buf, AXES, pairs)


def per_device(snapshots, panels, diag_inverse):
    local_count, order_size = snapshots.shape
    sections, blocks, width_block, _ = panels.shape
    devices = lax.axis_size(AXES)
    levels = (devices - 1).bit_length()
    pieces = snapshots.reshape(local_count, blocks, devices, width_block)
    arrived = lax.all_to_all(pieces, AXES, split_axis=2, concat_axis=0, tiled=True)
    remaining = jnp.transpose(
        arrived.reshape(devices * local_count, blocks, width_block), (1, 2, 0)
    )
    device = lax.axis_index(AXES)
    lead = remaining[0]
    low = panels[:, 0]

    after = [[None] * 3 for _ in range(sections)]
    first_hop = [None] * sections
    solved_all = [None] * sections
    settled = lead
    for section in range(sections):
        chain = settled
        if section >= 1:
            chain = chain - mm(low[section - 1], first_hop[section - 1])
        for back in (2, 3):
            if section - back >= 0:
                chain = chain - mm(low[section - back], after[section - back][1])
        solved = mm(diag_inverse[section], chain)
        buf = jnp.where(device == section, solved, jnp.zeros_like(solved))
        for level in range(levels):
            got = tree_round(buf, section, level, devices)
            if level == 0:
                first_hop[section] = got
            buf = buf + got
            if level < 3:
                after[section][level] = buf
        solved_all[section] = buf
        if section - 3 >= 0:
            settled = settled - mm(low[section - 3], after[section - 3][2])

    update = remaining
    for section in range(sections):
        update = update - jnp.einsum(
            "jrc,cs->jrs",
            panels[section],
            solved_all[section],
            precision=HI,
            preferred_element_type=jnp.float32,
        )
    stacked = jnp.stack(solved_all)
    own = lax.dynamic_index_in_dim(stacked, jnp.minimum(device, sections - 1), 0, keepdims=False)
    first = jnp.where(device < sections, own, update[0])
    return jnp.concatenate([first[None], update[1:]], axis=0)


def solution(mesh):
    in_specs = (P(AXES, None), P(None, None, AXES, None), P())
    out_specs = P(None, AXES, None)
    return jax.shard_map(
        per_device, mesh=mesh, in_specs=in_specs, out_specs=out_specs, check_vma=False
    )
```

```python
import jax
import jax.numpy as jnp
from jax import lax
from jax.sharding import PartitionSpec as P

AXES = ("row", "col")
HI = lax.Precision.HIGHEST


def mm(a, b):
    return jnp.dot(a, b, precision=HI, preferred_element_type=jnp.float32)


def transpose_in(pieces, devices):
    local_count, blocks, _, width_block = pieces.shape
    arrived = lax.all_to_all(pieces, AXES, split_axis=2, concat_axis=0, tiled=True)
    return jnp.transpose(arrived.reshape(devices * local_count, blocks, width_block), (1, 2, 0))


def per_device(snapshots, panels, diag_inverse):
    local_count, order_size = snapshots.shape
    sections, blocks, width_block, _ = panels.shape
    devices = lax.axis_size(AXES)
    cols = lax.axis_size("col")
    pieces = snapshots.reshape(local_count, blocks, devices, width_block)
    lead = transpose_in(pieces[:, :1], devices)[0]
    rest = transpose_in(pieces[:, 1:], devices)
    device = lax.axis_index(AXES)
    row = lax.axis_index("row")
    col = lax.axis_index("col")
    low = panels[:, 0]

    after = [[None] * 3 for _ in range(sections)]
    first_hop = [None] * sections
    own = jnp.zeros_like(lead)
    settled = lead
    for section in range(sections):
        chain = settled
        if section >= 1:
            chain = chain - mm(low[section - 1], first_hop[section - 1])
        for back in (2, 3):
            if section - back >= 0:
                chain = chain - mm(low[section - back], after[section - back][1])
        solved = mm(diag_inverse[section], chain)
        here = device == section
        own = jnp.where(here, solved, own)
        buf = jnp.where(here, solved, jnp.zeros_like(solved))
        for level in range(3):
            step = 2**level
            pairs = [
                (section + q, section + q + step)
                for q in range(step)
                if section + q + step < sections
            ]
            if pairs:
                got = lax.ppermute(buf, AXES, pairs)
                if level == 0:
                    first_hop[section] = got
                buf = buf + got
            after[section][level] = buf
        if section - 3 >= 0:
            settled = settled - mm(low[section - 3], after[section - 3][2])

    moved = lax.ppermute(own, AXES, [(k, k * cols + k) for k in range(1, sections)])
    spread = jnp.where(device == 0, own, moved)
    level = 1
    while level < cols:
        pairs = [
            (r * cols + (r + q) % cols, r * cols + (r + q + level) % cols)
            for r in range(sections)
            for q in range(level)
        ]
        spread = spread + lax.ppermute(spread, AXES, pairs)
        level *= 2
    whole = lax.all_gather(spread, "row", tiled=True)

    update = jnp.concatenate([lead[None], rest], axis=0)
    for section in range(sections):
        update = update - jnp.einsum(
            "jrc,cs->jrs",
            panels[section],
            whole[section * width_block:(section + 1) * width_block],
            precision=HI,
            preferred_element_type=jnp.float32,
        )
    first = jnp.where(device < sections, own, update[0])
    return jnp.concatenate([first[None], update[1:]], axis=0)


def solution(mesh):
    in_specs = (P(AXES, None), P(None, None, AXES, None), P())
    out_specs = P(None, AXES, None)
    return jax.shard_map(
        per_device, mesh=mesh, in_specs=in_specs, out_specs=out_specs, check_vma=False
    )
```

```python
import jax
import jax.numpy as jnp
from jax import lax
from jax.sharding import PartitionSpec as P

AXES = ("row", "col")
HI = lax.Precision.HIGHEST


def mm(a, b):
    return jnp.dot(a, b, precision=HI, preferred_element_type=jnp.float32)


def transpose_in(pieces, devices):
    local_count, blocks, _, width_block = pieces.shape
    arrived = lax.all_to_all(pieces, AXES, split_axis=2, concat_axis=0, tiled=True)
    return jnp.transpose(arrived.reshape(devices * local_count, blocks, width_block), (1, 2, 0))


def per_device(snapshots, panels, diag_inverse):
    local_count, order_size = snapshots.shape
    sections, blocks, width_block, _ = panels.shape
    devices = lax.axis_size(AXES)
    cols = lax.axis_size("col")
    pieces = snapshots.reshape(local_count, blocks, devices, width_block)
    lead = transpose_in(pieces[:, :1], devices)[0]
    rest = transpose_in(pieces[:, 1:], devices)
    device = lax.axis_index(AXES)
    row = lax.axis_index("row")
    col = lax.axis_index("col")
    low = panels[:, 0]

    after = [[None] * 3 for _ in range(sections)]
    first_hop = [None] * sections
    own = jnp.zeros_like(lead)
    settled = lead
    for section in range(sections):
        chain = settled
        if section >= 1:
            chain = chain - mm(low[section - 1], first_hop[section - 1])
        for back in (2, 3):
            if section - back >= 0:
                chain = chain - mm(low[section - back], after[section - back][1])
        solved = mm(diag_inverse[section], chain)
        here = device == section
        own = jnp.where(here, solved, own)
        buf = jnp.where(here, solved, jnp.zeros_like(solved))
        for level in range(3):
            step = 2**level
            pairs = [
                (section + q, section + q + step)
                for q in range(step)
                if section + q + step < sections
            ]
            if pairs:
                got = lax.ppermute(buf, AXES, pairs)
                if level == 0:
                    first_hop[section] = got
                buf = buf + got
            after[section][level] = buf
        if section - 3 >= 0:
            settled = settled - mm(low[section - 3], after[section - 3][2])

    rows = lax.axis_size("row")
    halves = cols // sections
    cut = width_block // rows
    down = lax.all_to_all(own.reshape(rows, cut, -1), "row", 0, 0, tiled=True)[0]
    part = cut // halves
    pieces_out = down.reshape(halves, part, -1)
    mine = pieces_out[0]
    for h in range(1, halves):
        pairs = [
            (r * cols + k, r * cols + k + h * sections)
            for r in range(rows)
            for k in range(sections)
        ]
        got = lax.ppermute(pieces_out[h], AXES, pairs)
        mine = jnp.where(col // sections == h, got, mine)
    gathered = lax.all_gather(mine, AXES, tiled=True)
    whole = (
        gathered.reshape(rows, halves, sections, part, -1)
        .transpose(2, 0, 1, 3, 4)
        .reshape(sections * width_block, -1)
    )

    update = jnp.concatenate([lead[None], rest], axis=0)
    for section in range(sections):
        update = update - jnp.einsum(
            "jrc,cs->jrs",
            panels[section],
            whole[section * width_block:(section + 1) * width_block],
            precision=HI,
            preferred_element_type=jnp.float32,
        )
    first = jnp.where(device < sections, own, update[0])
    return jnp.concatenate([first[None], update[1:]], axis=0)


def solution(mesh):
    in_specs = (P(AXES, None), P(None, None, AXES, None), P())
    out_specs = P(None, AXES, None)
    return jax.shard_map(
        per_device, mesh=mesh, in_specs=in_specs, out_specs=out_specs, check_vma=False
    )
```

```python
import jax
import jax.numpy as jnp
from jax import lax
from jax.sharding import PartitionSpec as P

AXES = ("row", "col")
HI = lax.Precision.HIGHEST


def mm(a, b):
    return jnp.dot(a, b, precision=HI, preferred_element_type=jnp.float32)


def transpose_in(pieces, devices):
    local_count, blocks, _, width_block = pieces.shape
    arrived = lax.all_to_all(pieces, AXES, split_axis=2, concat_axis=0, tiled=True)
    return jnp.transpose(arrived.reshape(devices * local_count, blocks, width_block), (1, 2, 0))


def per_device(snapshots, panels, diag_inverse):
    local_count, order_size = snapshots.shape
    sections, blocks, width_block, _ = panels.shape
    devices = lax.axis_size(AXES)
    cols = lax.axis_size("col")
    pieces = snapshots.reshape(local_count, blocks, devices, width_block)
    remaining = transpose_in(pieces, devices)
    lead = remaining[0]
    device = lax.axis_index(AXES)
    row = lax.axis_index("row")
    col = lax.axis_index("col")
    low = panels[:, 0]

    after = [[None] * 3 for _ in range(sections)]
    first_hop = [None] * sections
    own = jnp.zeros_like(lead)
    settled = lead
    for section in range(sections):
        chain = settled
        if section >= 1:
            chain = chain - mm(low[section - 1], first_hop[section - 1])
        for back in (2, 3):
            if section - back >= 0:
                chain = chain - mm(low[section - back], after[section - back][1])
        solved = mm(diag_inverse[section], chain)
        here = device == section
        own = jnp.where(here, solved, own)
        buf = jnp.where(here, solved, jnp.zeros_like(solved))
        for level in range(3):
            step = 2**level
            pairs = [
                (section + q, section + q + step)
                for q in range(step)
                if section + q + step < sections
            ]
            if pairs:
                got = lax.ppermute(buf, AXES, pairs)
                if level == 0:
                    first_hop[section] = got
                buf = buf + got
            after[section][level] = buf
        if section - 3 >= 0:
            settled = settled - mm(low[section - 3], after[section - 3][2])

    rows = lax.axis_size("row")
    halves = cols // sections
    cut = width_block // rows
    down = lax.all_to_all(own.reshape(rows, cut, -1), "row", 0, 0, tiled=True)[0]
    part = cut // halves
    pieces_out = down.reshape(halves, part, -1)
    mine = pieces_out[0]
    for h in range(1, halves):
        pairs = [
            (r * cols + k, r * cols + k + h * sections)
            for r in range(rows)
            for k in range(sections)
        ]
        got = lax.ppermute(pieces_out[h], AXES, pairs)
        mine = jnp.where(col // sections == h, got, mine)
    gathered = lax.all_gather(lax.all_gather(mine, "col", tiled=True), "row", tiled=True)
    whole = (
        gathered.reshape(rows, halves, sections, part, -1)
        .transpose(2, 0, 1, 3, 4)
        .reshape(sections * width_block, -1)
    )

    update = remaining
    for section in range(sections):
        update = update - jnp.einsum(
            "jrc,cs->jrs",
            panels[section],
            whole[section * width_block:(section + 1) * width_block],
            precision=HI,
            preferred_element_type=jnp.float32,
        )
    first = jnp.where(device < sections, own, update[0])
    return jnp.concatenate([first[None], update[1:]], axis=0)


def solution(mesh):
    in_specs = (P(AXES, None), P(None, None, AXES, None), P())
    out_specs = P(None, AXES, None)
    return jax.shard_map(
        per_device, mesh=mesh, in_specs=in_specs, out_specs=out_specs, check_vma=False
    )
```

```python
import jax
import jax.numpy as jnp
from jax import lax
from jax.sharding import PartitionSpec as P

AXES = ("row", "col")
HI = lax.Precision.HIGHEST


def mm(a, b):
    return jnp.dot(a, b, precision=HI, preferred_element_type=jnp.float32)


def transpose_in(pieces, devices):
    local_count, blocks, _, width_block = pieces.shape
    arrived = lax.all_to_all(pieces, AXES, split_axis=2, concat_axis=0, tiled=True)
    return jnp.transpose(arrived.reshape(devices * local_count, blocks, width_block), (1, 2, 0))


def per_device(snapshots, panels, diag_inverse):
    local_count, order_size = snapshots.shape
    sections, blocks, width_block, _ = panels.shape
    devices = lax.axis_size(AXES)
    cols = lax.axis_size("col")
    pieces = snapshots.reshape(local_count, blocks, devices, width_block)
    lead = transpose_in(pieces[:, :1], devices)[0]
    rest = transpose_in(pieces[:, 1:], devices)
    device = lax.axis_index(AXES)
    row = lax.axis_index("row")
    col = lax.axis_index("col")
    low = panels[:, 0]

    after = [[None] * 3 for _ in range(sections)]
    first_hop = [None] * sections
    own = jnp.zeros_like(lead)
    settled = lead
    for section in range(sections):
        chain = settled
        if section >= 1:
            chain = chain - mm(low[section - 1], first_hop[section - 1])
        for back in (2, 3):
            if section - back >= 0:
                chain = chain - mm(low[section - back], after[section - back][1])
        solved = mm(diag_inverse[section], chain)
        here = device == section
        own = jnp.where(here, solved, own)
        buf = jnp.where(here, solved, jnp.zeros_like(solved))
        for level in range(3):
            step = 2**level
            pairs = [
                (section + q, section + q + step)
                for q in range(step)
                if section + q + step < sections
            ]
            if pairs:
                got = lax.ppermute(buf, AXES, pairs)
                if level == 0:
                    first_hop[section] = got
                buf = buf + got
            after[section][level] = buf
        if section - 3 >= 0:
            settled = settled - mm(low[section - 3], after[section - 3][2])

    rows = lax.axis_size("row")
    halves = cols // sections
    cut = width_block // rows
    down = lax.all_to_all(own.reshape(rows, cut, -1), "row", 0, 0, tiled=True)[0]
    part = cut // halves
    pieces_out = down.reshape(halves, part, -1)
    mine = pieces_out[0]
    for h in range(1, halves):
        pairs = [
            (r * cols + k, r * cols + k + h * sections)
            for r in range(rows)
            for k in range(sections)
        ]
        got = lax.ppermute(pieces_out[h], AXES, pairs)
        mine = jnp.where(col // sections == h, got, mine)
    update = jnp.concatenate([lead[None], rest], axis=0)
    width = update.shape[-1]
    span = width // 2
    done = []
    for lo in range(0, width, span):
        gathered = lax.all_gather(mine[:, lo:lo + span], AXES, tiled=True)
        whole = (
            gathered.reshape(rows, halves, sections, part, span)
            .transpose(2, 0, 1, 3, 4)
            .reshape(sections * width_block, span)
        )
        half = update[..., lo:lo + span]
        for section in range(sections):
            half = half - jnp.einsum(
                "jrc,cs->jrs",
                panels[section],
                whole[section * width_block:(section + 1) * width_block],
                precision=lax.Precision.HIGH,
                preferred_element_type=jnp.float32,
            )
        done.append(half)
    update = jnp.concatenate(done, axis=-1)
    first = jnp.where(device < sections, own, update[0])
    return jnp.concatenate([first[None], update[1:]], axis=0)


def solution(mesh):
    in_specs = (P(AXES, None), P(None, None, AXES, None), P())
    out_specs = P(None, AXES, None)
    return jax.shard_map(
        per_device, mesh=mesh, in_specs=in_specs, out_specs=out_specs, check_vma=False
    )
```

```python
import jax
import jax.numpy as jnp
from jax import lax
from jax.sharding import PartitionSpec as P

AXES = ("row", "col")
HI = lax.Precision.HIGHEST


def mm(a, b):
    return jnp.dot(a, b, precision=HI, preferred_element_type=jnp.float32)


def transpose_in(pieces, devices):
    local_count, blocks, _, width_block = pieces.shape
    arrived = lax.all_to_all(pieces, AXES, split_axis=2, concat_axis=0, tiled=True)
    return jnp.transpose(arrived.reshape(devices * local_count, blocks, width_block), (1, 2, 0))


def per_device(snapshots, panels, diag_inverse):
    local_count, order_size = snapshots.shape
    sections, blocks, width_block, _ = panels.shape
    devices = lax.axis_size(AXES)
    cols = lax.axis_size("col")
    pieces = snapshots.reshape(local_count, blocks, devices, width_block)
    lead = transpose_in(pieces[:, :1], devices)[0]
    rest = transpose_in(pieces[:, 1:], devices)
    device = lax.axis_index(AXES)
    row = lax.axis_index("row")
    col = lax.axis_index("col")
    inverse = lax.dynamic_index_in_dim(
        diag_inverse, jnp.minimum(device, sections - 1), 0, keepdims=False
    )
    low = jnp.stack([mm(inverse, panels[k, 0]) for k in range(sections - 1)])

    after = [[None] * 3 for _ in range(sections)]
    first_hop = [None] * sections
    own = jnp.zeros_like(lead)
    settled = mm(inverse, lead)
    for section in range(sections):
        chain = settled
        if section >= 1:
            chain = chain - mm(low[section - 1], first_hop[section - 1])
        for back in (2, 3):
            if section - back >= 0:
                chain = chain - mm(low[section - back], after[section - back][1])
        solved = chain
        here = device == section
        own = jnp.where(here, solved, own)
        buf = jnp.where(here, solved, jnp.zeros_like(solved))
        for level in range(3):
            step = 2**level
            pairs = [
                (section + q, section + q + step)
                for q in range(step)
                if section + q + step < sections
            ]
            if pairs:
                got = lax.ppermute(buf, AXES, pairs)
                if level == 0:
                    first_hop[section] = got
                buf = buf + got
            after[section][level] = buf
        if section - 3 >= 0:
            settled = settled - mm(low[section - 3], after[section - 3][2])

    rows = lax.axis_size("row")
    halves = cols // sections
    cut = width_block // rows
    down = lax.all_to_all(own.reshape(rows, cut, -1), "row", 0, 0, tiled=True)[0]
    part = cut // halves
    pieces_out = down.reshape(halves, part, -1)
    mine = pieces_out[0]
    for h in range(1, halves):
        pairs = [
            (r * cols + k, r * cols + k + h * sections)
            for r in range(rows)
            for k in range(sections)
        ]
        got = lax.ppermute(pieces_out[h], AXES, pairs)
        mine = jnp.where(col // sections == h, got, mine)
    gathered = lax.all_gather(mine, AXES, tiled=True)
    whole = (
        gathered.reshape(rows, halves, sections, part, -1)
        .transpose(2, 0, 1, 3, 4)
        .reshape(sections * width_block, -1)
    )

    update = jnp.concatenate([lead[None], rest], axis=0)
    for section in range(sections):
        update = update - jnp.einsum(
            "jrc,cs->jrs",
            panels[section],
            whole[section * width_block:(section + 1) * width_block],
            precision=lax.Precision.HIGH,
            preferred_element_type=jnp.float32,
        )
    first = jnp.where(device < sections, own, update[0])
    return jnp.concatenate([first[None], update[1:]], axis=0)


def solution(mesh):
    in_specs = (P(AXES, None), P(None, None, AXES, None), P())
    out_specs = P(None, AXES, None)
    return jax.shard_map(
        per_device, mesh=mesh, in_specs=in_specs, out_specs=out_specs, check_vma=False
    )
```

```python
import jax
import jax.numpy as jnp
from jax import lax
from jax.sharding import PartitionSpec as P

AXES = ("row", "col")
HI = lax.Precision.HIGHEST


def mm(a, b):
    return jnp.dot(a, b, precision=HI, preferred_element_type=jnp.float32)


def transpose_in(pieces, devices):
    local_count, blocks, _, width_block = pieces.shape
    arrived = lax.all_to_all(pieces, AXES, split_axis=2, concat_axis=0, tiled=True)
    return jnp.transpose(arrived.reshape(devices * local_count, blocks, width_block), (1, 2, 0))


def per_device(snapshots, panels, diag_inverse):
    local_count, order_size = snapshots.shape
    sections, blocks, width_block, _ = panels.shape
    devices = lax.axis_size(AXES)
    cols = lax.axis_size("col")
    pieces = snapshots.reshape(local_count, blocks, devices, width_block)
    lead = transpose_in(pieces[:, :1], devices)[0]
    rest = transpose_in(pieces[:, 1:], devices)
    device = lax.axis_index(AXES)
    row = lax.axis_index("row")
    col = lax.axis_index("col")
    low = panels[:, 0]

    after = [[None] * 3 for _ in range(sections)]
    first_hop = [None] * sections
    own = jnp.zeros_like(lead)
    settled = lead
    for section in range(sections):
        chain = settled
        if section >= 1:
            chain = chain - mm(low[section - 1], first_hop[section - 1])
        for back in (2, 3):
            if section - back >= 0:
                chain = chain - mm(low[section - back], after[section - back][1])
        solved = mm(diag_inverse[section], chain)
        here = device == section
        own = jnp.where(here, solved, own)
        buf = jnp.where(here, solved, jnp.zeros_like(solved))
        for level in range(3):
            step = 2**level
            pairs = [
                (section + q, section + q + step)
                for q in range(step)
                if section + q + step < sections
            ]
            if pairs:
                got = lax.ppermute(buf, AXES, pairs)
                if level == 0:
                    first_hop[section] = got
                buf = buf + got
            after[section][level] = buf
        if section - 3 >= 0:
            settled = settled - mm(low[section - 3], after[section - 3][2])

    rows = lax.axis_size("row")
    halves = cols // sections
    cut = width_block // rows
    down = lax.all_to_all(own.reshape(rows, cut, -1), "row", 0, 0, tiled=True)[0]
    part = cut // halves
    pieces_out = down.reshape(halves, part, -1)
    mine = pieces_out[0]
    for h in range(1, halves):
        pairs = [
            (r * cols + k, r * cols + k + h * sections)
            for r in range(rows)
            for k in range(sections)
        ]
        got = lax.ppermute(pieces_out[h], AXES, pairs)
        mine = jnp.where(col // sections == h, got, mine)
    gathered = lax.all_gather(mine, AXES, tiled=True)
    whole = (
        gathered.reshape(rows, halves, sections, part, -1)
        .transpose(2, 0, 1, 3, 4)
        .reshape(sections * width_block, -1)
    )

    update = jnp.concatenate([lead[None], rest], axis=0)
    for section in range(sections):
        update = update - jnp.einsum(
            "jrc,cs->jrs",
            panels[section],
            whole[section * width_block:(section + 1) * width_block],
            precision=lax.Precision.HIGH,
            preferred_element_type=jnp.float32,
        )
    first = jnp.where(device < sections, own, update[0])
    return jnp.concatenate([first[None], update[1:]], axis=0)


def solution(mesh):
    in_specs = (P(AXES, None), P(None, None, AXES, None), P())
    out_specs = P(None, AXES, None)
    return jax.shard_map(
        per_device, mesh=mesh, in_specs=in_specs, out_specs=out_specs, check_vma=False
    )
```

```python
import jax
import jax.numpy as jnp
from jax import lax
from jax.sharding import PartitionSpec as P

AXES = ("row", "col")
HI = lax.Precision.HIGHEST


def mm(a, b):
    return jnp.dot(a, b, precision=HI, preferred_element_type=jnp.float32)


def transpose_in(pieces, devices):
    local_count, blocks, _, width_block = pieces.shape
    arrived = lax.all_to_all(pieces, AXES, split_axis=2, concat_axis=0, tiled=True)
    return jnp.transpose(arrived.reshape(devices * local_count, blocks, width_block), (1, 2, 0))


def per_device(snapshots, panels, diag_inverse):
    local_count, order_size = snapshots.shape
    sections, blocks, width_block, _ = panels.shape
    devices = lax.axis_size(AXES)
    cols = lax.axis_size("col")
    pieces = snapshots.reshape(local_count, blocks, devices, width_block)
    lead = transpose_in(pieces[:, :1], devices)[0]
    rest = transpose_in(pieces[:, 1:], devices)
    device = lax.axis_index(AXES)
    row = lax.axis_index("row")
    col = lax.axis_index("col")
    inverse = lax.dynamic_index_in_dim(
        diag_inverse, jnp.minimum(device, sections - 1), 0, keepdims=False
    )
    low = jnp.stack([mm(inverse, panels[k, 0]) for k in range(sections - 1)])

    after = [[None] * 3 for _ in range(sections)]
    first_hop = [None] * sections
    own = jnp.zeros_like(lead)
    settled = mm(inverse, lead)

    def tree_round(buf, root, level):
        step = 2**level
        pairs = [
            (root + q, root + q + step)
            for q in range(step)
            if root + q + step < sections
        ]
        if not pairs:
            return buf, None
        got = lax.ppermute(buf, AXES, pairs)
        return buf + got, got

    for section in range(sections):
        chain = settled
        if section >= 1:
            chain = chain - mm(low[section - 1], first_hop[section - 1])
        for back in (2, 3):
            if section - back >= 0:
                chain = chain - mm(low[section - back], after[section - back][1])
        solved = chain
        here = device == section
        own = jnp.where(here, solved, own)
        buf = jnp.where(here, solved, jnp.zeros_like(solved))
        after[section][0], first_hop[section] = tree_round(buf, section, 0)
        for level in (1, 2):
            root = section - level
            if root >= 0:
                held, _ = lax.optimization_barrier((after[root][level - 1], solved))
                after[root][level], _ = tree_round(held, root, level)
        if section - 3 >= 0:
            settled = settled - mm(low[section - 3], after[section - 3][2])

    rows = lax.axis_size("row")
    halves = cols // sections
    cut = width_block // rows
    down = lax.all_to_all(own.reshape(rows, cut, -1), "row", 0, 0, tiled=True)[0]
    part = cut // halves
    pieces_out = down.reshape(halves, part, -1)
    mine = pieces_out[0]
    for h in range(1, halves):
        pairs = [
            (r * cols + k, r * cols + k + h * sections)
            for r in range(rows)
            for k in range(sections)
        ]
        got = lax.ppermute(pieces_out[h], AXES, pairs)
        mine = jnp.where(col // sections == h, got, mine)
    gathered = lax.all_gather(mine, AXES, tiled=True)
    whole = (
        gathered.reshape(rows, halves, sections, part, -1)
        .transpose(2, 0, 1, 3, 4)
        .reshape(sections * width_block, -1)
    )

    update = jnp.concatenate([lead[None], rest], axis=0)
    for section in range(sections):
        update = update - jnp.einsum(
            "jrc,cs->jrs",
            panels[section],
            whole[section * width_block:(section + 1) * width_block],
            precision=lax.Precision.HIGH,
            preferred_element_type=jnp.float32,
        )
    first = jnp.where(device < sections, own, update[0])
    return jnp.concatenate([first[None], update[1:]], axis=0)


def solution(mesh):
    in_specs = (P(AXES, None), P(None, None, AXES, None), P())
    out_specs = P(None, AXES, None)
    return jax.shard_map(
        per_device, mesh=mesh, in_specs=in_specs, out_specs=out_specs, check_vma=False
    )
```

```python
import jax
import jax.numpy as jnp
from jax import lax
from jax.sharding import PartitionSpec as P

AXES = ("row", "col")
HI = lax.Precision.HIGHEST


def mm(a, b, precision=HI):
    return jnp.dot(a, b, precision=precision, preferred_element_type=jnp.float32)


def mm3(a, b):
    return mm(a, b, lax.Precision.HIGH)


def transpose_in(pieces, devices):
    local_count, blocks, _, width_block = pieces.shape
    arrived = lax.all_to_all(pieces, AXES, split_axis=2, concat_axis=0, tiled=True)
    return jnp.transpose(arrived.reshape(devices * local_count, blocks, width_block), (1, 2, 0))


def per_device(snapshots, panels, diag_inverse):
    local_count, order_size = snapshots.shape
    sections, blocks, width_block, _ = panels.shape
    devices = lax.axis_size(AXES)
    cols = lax.axis_size("col")
    pieces = snapshots.reshape(local_count, blocks, devices, width_block)
    lead = transpose_in(pieces[:, :1], devices)[0]
    rest = transpose_in(pieces[:, 1:], devices)
    device = lax.axis_index(AXES)
    row = lax.axis_index("row")
    col = lax.axis_index("col")
    inverse = lax.dynamic_index_in_dim(
        diag_inverse, jnp.minimum(device, sections - 1), 0, keepdims=False
    )
    low = jnp.stack([mm3(inverse, panels[k, 0]) for k in range(sections - 1)])

    after = [[None] * 3 for _ in range(sections)]
    received = [[None] * 3 for _ in range(sections)]
    own = jnp.zeros_like(lead)
    settled = mm3(inverse, lead)

    def tree_round(buf, root, level):
        step = 2**level
        pairs = [
            (root + q, root + q + step)
            for q in range(step)
            if root + q + step < sections
        ]
        if not pairs:
            return buf, None
        got = lax.ppermute(buf, AXES, pairs)
        return buf + got, got

    for section in range(sections):
        chain = settled
        if section >= 1:
            chain = chain - mm3(low[section - 1], received[section - 1][0])
        for back in (2, 3):
            if section - back >= 0:
                chain = chain - mm3(low[section - back], received[section - back][1])
        solved = chain
        here = device == section
        own = jnp.where(here, solved, own)
        buf = jnp.where(here, solved, jnp.zeros_like(solved))
        after[section][0], received[section][0] = tree_round(buf, section, 0)
        for level in (1, 2):
            root = section - level
            if root >= 0:
                held, _ = lax.optimization_barrier((after[root][level - 1], solved))
                after[root][level], received[root][level] = tree_round(held, root, level)
        if section - 3 >= 0 and received[section - 3][2] is not None:
            settled = settled - mm3(low[section - 3], received[section - 3][2])

    rows = lax.axis_size("row")
    halves = cols // sections
    cut = width_block // rows
    down = lax.all_to_all(own.reshape(rows, cut, -1), "row", 0, 0, tiled=True)[0]
    part = cut // halves
    pieces_out = down.reshape(halves, part, -1)
    mine = pieces_out[0]
    for h in range(1, halves):
        pairs = [
            (r * cols + k, r * cols + k + h * sections)
            for r in range(rows)
            for k in range(sections)
        ]
        got = lax.ppermute(pieces_out[h], AXES, pairs)
        mine = jnp.where(col // sections == h, got, mine)
    gathered = lax.all_gather(mine, AXES, tiled=True)
    whole = (
        gathered.reshape(rows, halves, sections, part, -1)
        .transpose(2, 0, 1, 3, 4)
        .reshape(sections * width_block, -1)
    )

    update = jnp.concatenate([lead[None], rest], axis=0)
    for section in range(sections):
        update = update - jnp.einsum(
            "jrc,cs->jrs",
            panels[section],
            whole[section * width_block:(section + 1) * width_block],
            precision=lax.Precision.HIGH,
            preferred_element_type=jnp.float32,
        )
    first = jnp.where(device < sections, own, update[0])
    return jnp.concatenate([first[None], update[1:]], axis=0)


def solution(mesh):
    in_specs = (P(AXES, None), P(None, None, AXES, None), P())
    out_specs = P(None, AXES, None)
    return jax.shard_map(
        per_device, mesh=mesh, in_specs=in_specs, out_specs=out_specs, check_vma=False
    )
```

```python
import jax
import jax.numpy as jnp
from jax import lax
from jax.sharding import PartitionSpec as P

AXES = ("row", "col")
HI = lax.Precision.HIGHEST


def mm(a, b):
    return jnp.dot(a, b, precision=HI, preferred_element_type=jnp.float32)


def transpose_in(pieces, devices):
    local_count, blocks, _, width_block = pieces.shape
    arrived = lax.all_to_all(pieces, AXES, split_axis=2, concat_axis=0, tiled=True)
    return jnp.transpose(arrived.reshape(devices * local_count, blocks, width_block), (1, 2, 0))


def per_device(snapshots, panels, diag_inverse):
    local_count, order_size = snapshots.shape
    sections, blocks, width_block, _ = panels.shape
    devices = lax.axis_size(AXES)
    cols = lax.axis_size("col")
    pieces = snapshots.reshape(local_count, blocks, devices, width_block)
    lead = transpose_in(pieces[:, :1], devices)[0]
    rest = transpose_in(pieces[:, 1:], devices)
    device = lax.axis_index(AXES)
    row = lax.axis_index("row")
    col = lax.axis_index("col")
    inverse = lax.dynamic_index_in_dim(
        diag_inverse, jnp.minimum(device, sections - 1), 0, keepdims=False
    )
    low = jnp.stack([mm(inverse, panels[k, 0]) for k in range(sections - 1)])

    after = [[None] * 3 for _ in range(sections)]
    first_hop = [None] * sections
    own = jnp.zeros_like(lead)
    settled = mm(inverse, lead)

    def tree_round(buf, root, level):
        step = 2**level
        pairs = [
            (root + q, root + q + step)
            for q in range(step)
            if root + q + step < sections
        ]
        if not pairs:
            return buf, None
        got = lax.ppermute(buf, AXES, pairs)
        return buf + got, got

    for section in range(sections):
        chain = settled
        if section >= 1:
            chain = chain - mm(low[section - 1], first_hop[section - 1])
        for back in (2, 3):
            if section - back >= 0:
                chain = chain - mm(low[section - back], after[section - back][1])
        solved = chain
        here = device == section
        own = jnp.where(here, solved, own)
        buf = jnp.where(here, solved, jnp.zeros_like(solved))
        after[section][0], first_hop[section] = tree_round(buf, section, 0)
        for level in (1, 2):
            root = section - level
            if root >= 0:
                held, _ = lax.optimization_barrier((after[root][level - 1], solved))
                after[root][level], _ = tree_round(held, root, level)
        if section - 3 >= 0:
            settled = settled - mm(low[section - 3], after[section - 3][2])

    rows = lax.axis_size("row")
    chunk = width_block // cols
    across = lax.all_to_all(own.reshape(cols, chunk, -1), "col", 0, 0, tiled=True)
    mine = lax.all_to_all(across[:rows], "row", 0, 0, tiled=True)[0]
    whole = lax.all_gather(mine, AXES, tiled=True)

    update = jnp.concatenate([lead[None], rest], axis=0)
    for section in range(sections):
        update = update - jnp.einsum(
            "jrc,cs->jrs",
            panels[section],
            whole[section * width_block:(section + 1) * width_block],
            precision=lax.Precision.HIGH,
            preferred_element_type=jnp.float32,
        )
    first = jnp.where(device < sections, own, update[0])
    return jnp.concatenate([first[None], update[1:]], axis=0)


def solution(mesh):
    in_specs = (P(AXES, None), P(None, None, AXES, None), P())
    out_specs = P(None, AXES, None)
    return jax.shard_map(
        per_device, mesh=mesh, in_specs=in_specs, out_specs=out_specs, check_vma=False
    )
```

```python
import jax
import jax.numpy as jnp
from jax import lax
from jax.sharding import PartitionSpec as P

AXES = ("row", "col")
HI = lax.Precision.HIGHEST


def mm(a, b):
    return jnp.dot(a, b, precision=HI, preferred_element_type=jnp.float32)


def transpose_in(pieces, devices):
    local_count, blocks, _, width_block = pieces.shape
    arrived = lax.all_to_all(pieces, AXES, split_axis=2, concat_axis=0, tiled=True)
    return jnp.transpose(arrived.reshape(devices * local_count, blocks, width_block), (1, 2, 0))


def per_device(snapshots, panels, diag_inverse):
    local_count, order_size = snapshots.shape
    sections, blocks, width_block, _ = panels.shape
    devices = lax.axis_size(AXES)
    cols = lax.axis_size("col")
    pieces = snapshots.reshape(local_count, blocks, devices, width_block)
    remaining = transpose_in(pieces, devices)
    lead = remaining[0]
    device = lax.axis_index(AXES)
    row = lax.axis_index("row")
    col = lax.axis_index("col")
    inverse = lax.dynamic_index_in_dim(
        diag_inverse, jnp.minimum(device, sections - 1), 0, keepdims=False
    )
    low = jnp.stack([mm(inverse, panels[k, 0]) for k in range(sections - 1)])

    after = [[None] * 3 for _ in range(sections)]
    first_hop = [None] * sections
    own = jnp.zeros_like(lead)
    settled = mm(inverse, lead)
    for section in range(sections):
        chain = settled
        if section >= 1:
            chain = chain - mm(low[section - 1], first_hop[section - 1])
        for back in (2, 3):
            if section - back >= 0:
                chain = chain - mm(low[section - back], after[section - back][1])
        solved = chain
        here = device == section
        own = jnp.where(here, solved, own)
        buf = jnp.where(here, solved, jnp.zeros_like(solved))
        for level in range(3):
            step = 2**level
            pairs = [
                (section + q, section + q + step)
                for q in range(step)
                if section + q + step < sections
            ]
            if pairs:
                got = lax.ppermute(buf, AXES, pairs)
                if level == 0:
                    first_hop[section] = got
                buf = buf + got
            after[section][level] = buf
        if section - 3 >= 0:
            settled = settled - mm(low[section - 3], after[section - 3][2])

    rows = lax.axis_size("row")
    halves = cols // sections
    cut = width_block // rows
    down = lax.all_to_all(own.reshape(rows, cut, -1), "row", 0, 0, tiled=True)[0]
    part = cut // halves
    pieces_out = down.reshape(halves, part, -1)
    mine = pieces_out[0]
    for h in range(1, halves):
        pairs = [
            (r * cols + k, r * cols + k + h * sections)
            for r in range(rows)
            for k in range(sections)
        ]
        got = lax.ppermute(pieces_out[h], AXES, pairs)
        mine = jnp.where(col // sections == h, got, mine)
    gathered = lax.all_gather(mine, AXES, tiled=True)
    whole = (
        gathered.reshape(rows, halves, sections, part, -1)
        .transpose(2, 0, 1, 3, 4)
        .reshape(sections * width_block, -1)
    )

    update = remaining
    for section in range(sections):
        update = update - jnp.einsum(
            "jrc,cs->jrs",
            panels[section],
            whole[section * width_block:(section + 1) * width_block],
            precision=lax.Precision.HIGH,
            preferred_element_type=jnp.float32,
        )
    first = jnp.where(device < sections, own, update[0])
    return jnp.concatenate([first[None], update[1:]], axis=0)


def solution(mesh):
    in_specs = (P(AXES, None), P(None, None, AXES, None), P())
    out_specs = P(None, AXES, None)
    return jax.shard_map(
        per_device, mesh=mesh, in_specs=in_specs, out_specs=out_specs, check_vma=False
    )
```

```python
import jax
import jax.numpy as jnp
from jax import lax
from jax.sharding import PartitionSpec as P

AXES = ("row", "col")
HI = lax.Precision.HIGHEST


def mm(a, b):
    return jnp.dot(a, b, precision=HI, preferred_element_type=jnp.float32)


def transpose_in(pieces, devices):
    local_count, blocks, _, width_block = pieces.shape
    arrived = lax.all_to_all(pieces, AXES, split_axis=2, concat_axis=0, tiled=True)
    return jnp.transpose(arrived.reshape(devices * local_count, blocks, width_block), (1, 2, 0))


def per_device(snapshots, panels, diag_inverse):
    local_count, order_size = snapshots.shape
    sections, blocks, width_block, _ = panels.shape
    devices = lax.axis_size(AXES)
    cols = lax.axis_size("col")
    pieces = snapshots.reshape(local_count, blocks, devices, width_block)
    lead = transpose_in(pieces[:, :1], devices)[0]
    rest = transpose_in(pieces[:, 1:], devices)
    device = lax.axis_index(AXES)
    row = lax.axis_index("row")
    col = lax.axis_index("col")
    inverse = lax.dynamic_index_in_dim(
        diag_inverse, jnp.minimum(device, sections - 1), 0, keepdims=False
    )
    low = jnp.stack([mm(inverse, panels[k, 0]) for k in range(sections - 1)])

    after = [[None] * 3 for _ in range(sections)]
    first_hop = [None] * sections
    own = jnp.zeros_like(lead)
    settled = mm(inverse, lead)
    for section in range(sections):
        chain = settled
        if section >= 1:
            chain = chain - mm(low[section - 1], first_hop[section - 1])
        for back in (2, 3):
            if section - back >= 0:
                chain = chain - mm(low[section - back], after[section - back][1])
        solved = chain
        here = device == section
        own = jnp.where(here, solved, own)
        buf = jnp.where(here, solved, jnp.zeros_like(solved))
        for level in range(3):
            step = 2**level
            pairs = [
                (section + q, section + q + step)
                for q in range(step)
                if section + q + step < sections
            ]
            if pairs:
                got = lax.ppermute(buf, "col", pairs)
                if level == 0:
                    first_hop[section] = got
                buf = buf + got
            after[section][level] = buf
        if section - 3 >= 0:
            settled = settled - mm(low[section - 3], after[section - 3][2])

    rows = lax.axis_size("row")
    halves = cols // sections
    cut = width_block // rows
    down = lax.all_to_all(own.reshape(rows, cut, -1), "row", 0, 0, tiled=True)[0]
    part = cut // halves
    pieces_out = down.reshape(halves, part, -1)
    mine = pieces_out[0]
    for h in range(1, halves):
        pairs = [(k, k + h * sections) for k in range(sections)]
        got = lax.ppermute(pieces_out[h], "col", pairs)
        mine = jnp.where(col // sections == h, got, mine)
    gathered = lax.all_gather(mine, AXES, tiled=True)
    whole = (
        gathered.reshape(rows, halves, sections, part, -1)
        .transpose(2, 0, 1, 3, 4)
        .reshape(sections * width_block, -1)
    )

    update = jnp.concatenate([lead[None], rest], axis=0)
    for section in range(sections):
        update = update - jnp.einsum(
            "jrc,cs->jrs",
            panels[section],
            whole[section * width_block:(section + 1) * width_block],
            precision=lax.Precision.HIGH,
            preferred_element_type=jnp.float32,
        )
    first = jnp.where(device < sections, own, update[0])
    return jnp.concatenate([first[None], update[1:]], axis=0)


def solution(mesh):
    in_specs = (P(AXES, None), P(None, None, AXES, None), P())
    out_specs = P(None, AXES, None)
    return jax.shard_map(
        per_device, mesh=mesh, in_specs=in_specs, out_specs=out_specs, check_vma=False
    )
```

```python
import jax
import jax.numpy as jnp
from jax import lax
from jax.sharding import PartitionSpec as P

AXES = ("row", "col")
HI = lax.Precision.HIGHEST


def mm(a, b):
    return jnp.dot(a, b, precision=HI, preferred_element_type=jnp.float32)


def transpose_in(pieces, devices):
    local_count, blocks, _, width_block = pieces.shape
    arrived = lax.all_to_all(pieces, AXES, split_axis=2, concat_axis=0, tiled=True)
    return jnp.transpose(arrived.reshape(devices * local_count, blocks, width_block), (1, 2, 0))


def per_device(snapshots, panels, diag_inverse):
    local_count, order_size = snapshots.shape
    sections, blocks, width_block, _ = panels.shape
    devices = lax.axis_size(AXES)
    cols = lax.axis_size("col")
    pieces = snapshots.reshape(local_count, blocks, devices, width_block)
    lead = transpose_in(pieces[:, :1], devices)[0]
    rest = transpose_in(pieces[:, 1:], devices)
    device = lax.axis_index(AXES)
    row = lax.axis_index("row")
    col = lax.axis_index("col")
    inverse = lax.dynamic_index_in_dim(
        diag_inverse, jnp.minimum(device, sections - 1), 0, keepdims=False
    )
    low = jnp.stack([mm(inverse, panels[k, 0]) for k in range(sections - 1)])

    after = [[None] * 3 for _ in range(sections)]
    first_hop = [None] * sections
    own = jnp.zeros_like(lead)
    settled = mm(inverse, lead)
    for section in range(sections):
        chain = settled
        if section >= 1:
            chain = chain - mm(low[section - 1], first_hop[section - 1])
        for back in (2, 3):
            if section - back >= 0:
                chain = chain - mm(low[section - back], after[section - back][1])
        solved = chain
        here = device == section
        own = jnp.where(here, solved, own)
        buf = jnp.where(here, solved, jnp.zeros_like(solved))
        for level in range(3):
            step = 2**level
            pairs = [
                (section + q, section + q + step)
                for q in range(step)
                if section + q + step < sections
            ]
            if pairs:
                got = lax.ppermute(buf, AXES, pairs)
                if level == 0:
                    first_hop[section] = got
                buf = buf + got
            after[section][level] = buf
        if section - 3 >= 0:
            settled = settled - mm(low[section - 3], after[section - 3][2])

    rows = lax.axis_size("row")
    halves = cols // sections
    cut = width_block // rows
    down = lax.all_to_all(own.reshape(rows, cut, -1), "row", 0, 0, tiled=True)[0]
    part = cut // halves
    pieces_out = down.reshape(halves, part, -1)
    mine = pieces_out[0]
    for h in range(1, halves):
        pairs = [
            (r * cols + k, r * cols + k + h * sections)
            for r in range(rows)
            for k in range(sections)
        ]
        got = lax.ppermute(pieces_out[h], AXES, pairs)
        mine = jnp.where(col // sections == h, got, mine)
    gathered = lax.all_gather(mine, AXES, tiled=True)
    whole = (
        gathered.reshape(rows, halves, sections, part, -1)
        .transpose(2, 0, 1, 3, 4)
        .reshape(sections * width_block, -1)
    )

    update = jnp.concatenate([lead[None], rest], axis=0)
    update = update - jnp.einsum(
        "kjrc,kcs->jrs",
        panels,
        whole.reshape(sections, width_block, -1),
        precision=lax.Precision.HIGH,
        preferred_element_type=jnp.float32,
    )
    first = jnp.where(device < sections, own, update[0])
    return jnp.concatenate([first[None], update[1:]], axis=0)


def solution(mesh):
    in_specs = (P(AXES, None), P(None, None, AXES, None), P())
    out_specs = P(None, AXES, None)
    return jax.shard_map(
        per_device, mesh=mesh, in_specs=in_specs, out_specs=out_specs, check_vma=False
    )
```

```python
import jax
import jax.numpy as jnp
from jax import lax
from jax.sharding import PartitionSpec as P

AXES = ("row", "col")
HI = lax.Precision.HIGHEST


def mm(a, b):
    return jnp.dot(a, b, precision=HI, preferred_element_type=jnp.float32)


def transpose_in(pieces, devices):
    local_count, blocks, _, width_block = pieces.shape
    arrived = lax.all_to_all(pieces, AXES, split_axis=2, concat_axis=0, tiled=True)
    return jnp.transpose(arrived.reshape(devices * local_count, blocks, width_block), (1, 2, 0))


def per_device(snapshots, panels, diag_inverse):
    local_count, order_size = snapshots.shape
    sections, blocks, width_block, _ = panels.shape
    devices = lax.axis_size(AXES)
    cols = lax.axis_size("col")
    pieces = snapshots.reshape(local_count, blocks, devices, width_block)
    lead = transpose_in(pieces[:, :1], devices)[0]
    rest = transpose_in(pieces[:, 1:], devices)
    device = lax.axis_index(AXES)
    row = lax.axis_index("row")
    col = lax.axis_index("col")
    inverse = lax.dynamic_index_in_dim(
        diag_inverse, jnp.minimum(device, sections - 1), 0, keepdims=False
    )
    low = jnp.stack([mm(inverse, panels[k, 0]) for k in range(sections - 1)])

    after = [[None] * 3 for _ in range(sections)]
    first_hop = [None] * sections
    own = jnp.zeros_like(lead)
    settled = mm(inverse, lead)
    for section in range(sections):
        chain = settled
        if section >= 1:
            chain = chain - mm(low[section - 1], first_hop[section - 1])
        for back in (2, 3):
            if section - back >= 0:
                chain = chain - mm(low[section - back], after[section - back][1])
        solved = chain
        here = device == section
        own = jnp.where(here, solved, own)
        buf = jnp.where(here, solved, jnp.zeros_like(solved))
        for level in range(3):
            step = 2**level
            pairs = [
                (section + q, section + q + step)
                for q in range(step)
                if section + q + step < sections
            ]
            if pairs:
                got = lax.ppermute(buf, AXES, pairs)
                if level == 0:
                    first_hop[section] = got
                buf = buf + got
            after[section][level] = buf
        if section - 3 >= 0:
            settled = settled - mm(low[section - 3], after[section - 3][2])

    rows = lax.axis_size("row")
    halves = cols // sections
    cut = width_block // rows
    down = lax.all_to_all(own.reshape(rows, cut, -1), "row", 0, 0, tiled=True)[0]
    part = cut // halves
    pieces_out = down.reshape(halves, part, -1)
    mine = pieces_out[0]
    for h in range(1, halves):
        pairs = [
            (r * cols + k, r * cols + k + h * sections)
            for r in range(rows)
            for k in range(sections)
        ]
        got = lax.ppermute(pieces_out[h], AXES, pairs)
        mine = jnp.where(col // sections == h, got, mine)
    gathered = lax.all_gather(mine, AXES, tiled=True)

    update = jnp.concatenate([lead[None], rest], axis=0)
    update = update - jnp.einsum(
        "kjwrht,rhkts->jws",
        panels.reshape(sections, blocks, width_block, rows, halves, part),
        gathered.reshape(rows, halves, sections, part, -1),
        precision=lax.Precision.HIGH,
        preferred_element_type=jnp.float32,
    )
    first = jnp.where(device < sections, own, update[0])
    return jnp.concatenate([first[None], update[1:]], axis=0)


def solution(mesh):
    in_specs = (P(AXES, None), P(None, None, AXES, None), P())
    out_specs = P(None, AXES, None)
    return jax.shard_map(
        per_device, mesh=mesh, in_specs=in_specs, out_specs=out_specs, check_vma=False
    )
```

```python
import jax
import jax.numpy as jnp
from jax import lax
from jax.sharding import PartitionSpec as P

AXES = ("row", "col")
HI = lax.Precision.HIGHEST


def mm(a, b):
    return jnp.dot(a, b, precision=HI, preferred_element_type=jnp.float32)


def transpose_in(pieces, devices):
    local_count, blocks, _, width_block = pieces.shape
    arrived = lax.all_to_all(pieces, AXES, split_axis=2, concat_axis=0, tiled=True)
    return jnp.transpose(arrived.reshape(devices * local_count, blocks, width_block), (1, 2, 0))


def per_device(snapshots, panels, diag_inverse):
    local_count, order_size = snapshots.shape
    sections, blocks, width_block, _ = panels.shape
    devices = lax.axis_size(AXES)
    cols = lax.axis_size("col")
    pieces = snapshots.reshape(local_count, blocks, devices, width_block)
    lead = transpose_in(pieces[:, :1], devices)[0]
    rest = transpose_in(pieces[:, 1:], devices)
    device = lax.axis_index(AXES)
    row = lax.axis_index("row")
    col = lax.axis_index("col")
    inverse = lax.dynamic_index_in_dim(
        diag_inverse, jnp.minimum(device, sections - 1), 0, keepdims=False
    )
    low = jnp.stack([mm(inverse, panels[k, 0]) for k in range(sections - 1)])

    received = [[None] * 3 for _ in range(sections)]
    own = jnp.zeros_like(lead)
    settled = mm(inverse, lead)
    for section in range(sections):
        chain = settled
        if section >= 1:
            chain = chain - mm(low[section - 1], received[section - 1][0])
        for back in (2, 3):
            if section - back >= 0:
                chain = chain - mm(low[section - back], received[section - back][1])
        solved = chain
        here = device == section
        own = jnp.where(here, solved, own)
        buf = jnp.where(here, solved, jnp.zeros_like(solved))
        for level in range(3):
            step = 2**level
            pairs = [
                (section + q, section + q + step)
                for q in range(step)
                if section + q + step < sections
            ]
            if pairs:
                got = lax.ppermute(buf, AXES, pairs)
                received[section][level] = got
                if level < 2:
                    buf = buf + got
        if section - 3 >= 0 and received[section - 3][2] is not None:
            settled = settled - mm(low[section - 3], received[section - 3][2])

    rows = lax.axis_size("row")
    halves = cols // sections
    cut = width_block // rows
    down = lax.all_to_all(own.reshape(rows, cut, -1), "row", 0, 0, tiled=True)[0]
    part = cut // halves
    pieces_out = down.reshape(halves, part, -1)
    mine = pieces_out[0]
    for h in range(1, halves):
        pairs = [
            (r * cols + k, r * cols + k + h * sections)
            for r in range(rows)
            for k in range(sections)
        ]
        got = lax.ppermute(pieces_out[h], AXES, pairs)
        mine = jnp.where(col // sections == h, got, mine)
    gathered = lax.all_gather(mine, AXES, tiled=True)

    update = jnp.concatenate([lead[None], rest], axis=0)
    update = update - jnp.einsum(
        "kjwrht,rhkts->jws",
        panels.reshape(sections, blocks, width_block, rows, halves, part),
        gathered.reshape(rows, halves, sections, part, -1),
        precision=lax.Precision.HIGH,
        preferred_element_type=jnp.float32,
    )
    first = jnp.where(device < sections, own, update[0])
    return jnp.concatenate([first[None], update[1:]], axis=0)


def solution(mesh):
    in_specs = (P(AXES, None), P(None, None, AXES, None), P())
    out_specs = P(None, AXES, None)
    return jax.shard_map(
        per_device, mesh=mesh, in_specs=in_specs, out_specs=out_specs, check_vma=False
    )
```

```python
import jax
import jax.numpy as jnp
from jax import lax
from jax.sharding import PartitionSpec as P

AXES = ("row", "col")
HI = lax.Precision.HIGHEST


def mm(a, b):
    return jnp.dot(a, b, precision=HI, preferred_element_type=jnp.float32)


def transpose_in(pieces, devices):
    local_count, blocks, _, width_block = pieces.shape
    arrived = lax.all_to_all(pieces, AXES, split_axis=2, concat_axis=0, tiled=True)
    return jnp.transpose(arrived.reshape(devices * local_count, blocks, width_block), (1, 2, 0))


def per_device(snapshots, panels, diag_inverse):
    local_count, order_size = snapshots.shape
    sections, blocks, width_block, _ = panels.shape
    devices = lax.axis_size(AXES)
    cols = lax.axis_size("col")
    pieces = snapshots.reshape(local_count, blocks, devices, width_block)
    lead = transpose_in(pieces[:, :1], devices)[0]
    rest = transpose_in(pieces[:, 1:], devices)
    device = lax.axis_index(AXES)
    row = lax.axis_index("row")
    col = lax.axis_index("col")
    inverse = lax.dynamic_index_in_dim(
        diag_inverse, jnp.minimum(device, sections - 1), 0, keepdims=False
    )
    low = jnp.stack([jnp.dot(inverse, panels[k, 0], precision=lax.Precision.HIGH, preferred_element_type=jnp.float32) for k in range(sections - 1)])

    after = [[None] * 3 for _ in range(sections)]
    first_hop = [None] * sections
    own = jnp.zeros_like(lead)
    settled = jnp.dot(inverse, lead, precision=lax.Precision.HIGH, preferred_element_type=jnp.float32)
    for section in range(sections):
        chain = settled
        if section >= 1:
            chain = chain - mm(low[section - 1], first_hop[section - 1])
        for back in (2, 3):
            if section - back >= 0:
                chain = chain - mm(low[section - back], after[section - back][1])
        solved = chain
        here = device == section
        own = jnp.where(here, solved, own)
        buf = jnp.where(here, solved, jnp.zeros_like(solved))
        for level in range(3):
            step = 2**level
            pairs = [
                (section + q, section + q + step)
                for q in range(step)
                if section + q + step < sections
            ]
            if pairs:
                got = lax.ppermute(buf, AXES, pairs)
                if level == 0:
                    first_hop[section] = got
                buf = buf + got
            after[section][level] = buf
        if section - 3 >= 0:
            settled = settled - mm(low[section - 3], after[section - 3][2])

    rows = lax.axis_size("row")
    halves = cols // sections
    cut = width_block // rows
    down = lax.all_to_all(own.reshape(rows, cut, -1), "row", 0, 0, tiled=True)[0]
    part = cut // halves
    pieces_out = down.reshape(halves, part, -1)
    mine = pieces_out[0]
    for h in range(1, halves):
        pairs = [
            (r * cols + k, r * cols + k + h * sections)
            for r in range(rows)
            for k in range(sections)
        ]
        got = lax.ppermute(pieces_out[h], AXES, pairs)
        mine = jnp.where(col // sections == h, got, mine)
    gathered = lax.all_gather(mine, AXES, tiled=True)

    update = jnp.concatenate([lead[None], rest], axis=0)
    update = update - jnp.einsum(
        "kjwrht,rhkts->jws",
        panels.reshape(sections, blocks, width_block, rows, halves, part),
        gathered.reshape(rows, halves, sections, part, -1),
        precision=lax.Precision.HIGH,
        preferred_element_type=jnp.float32,
    )
    first = jnp.where(device < sections, own, update[0])
    return jnp.concatenate([first[None], update[1:]], axis=0)


def solution(mesh):
    in_specs = (P(AXES, None), P(None, None, AXES, None), P())
    out_specs = P(None, AXES, None)
    return jax.shard_map(
        per_device, mesh=mesh, in_specs=in_specs, out_specs=out_specs, check_vma=False
    )
```

```python
import jax
import jax.numpy as jnp
from jax import lax
from jax.sharding import PartitionSpec as P

AXES = ("row", "col")
HI = lax.Precision.HIGHEST


def mm(a, b):
    return jnp.dot(a, b, precision=HI, preferred_element_type=jnp.float32)


def transpose_in(pieces, devices):
    local_count, blocks, _, width_block = pieces.shape
    arrived = lax.all_to_all(pieces, AXES, split_axis=2, concat_axis=0, tiled=True)
    return jnp.transpose(arrived.reshape(devices * local_count, blocks, width_block), (1, 2, 0))


def per_device(snapshots, panels, diag_inverse):
    local_count, order_size = snapshots.shape
    sections, blocks, width_block, _ = panels.shape
    devices = lax.axis_size(AXES)
    cols = lax.axis_size("col")
    pieces = snapshots.reshape(local_count, blocks, devices, width_block)
    lead = transpose_in(pieces[:, :1], devices)[0]
    rest = transpose_in(pieces[:, 1:], devices)
    device = lax.axis_index(AXES)
    row = lax.axis_index("row")
    col = lax.axis_index("col")
    inverse = lax.dynamic_index_in_dim(
        diag_inverse, jnp.minimum(device, sections - 1), 0, keepdims=False
    )
    low = jnp.stack([mm(inverse, panels[k, 0]) for k in range(sections - 1)])

    after = [[None] * 3 for _ in range(sections)]
    first_hop = [None] * sections
    own = jnp.zeros_like(lead)
    settled = mm(inverse, lead)
    for section in range(sections):
        chain = settled
        if section >= 1:
            chain = chain - mm(low[section - 1], first_hop[section - 1])
        for back in (2, 3):
            if section - back >= 0:
                chain = chain - mm(low[section - back], after[section - back][1])
        solved = chain
        here = device == section
        own = jnp.where(here, solved, own)
        buf = jnp.where(here, solved, jnp.zeros_like(solved))
        for level in range(3):
            step = 2**level
            pairs = [
                (section + q, section + q + step)
                for q in range(step)
                if section + q + step < sections
            ]
            if pairs:
                got = lax.ppermute(buf, AXES, pairs)
                if level == 0:
                    first_hop[section] = got
                buf = buf + got
            after[section][level] = buf
        if section - 3 >= 0:
            settled = settled - mm(low[section - 3], after[section - 3][2])

    rows = lax.axis_size("row")
    halves = cols // sections
    half_rows = width_block // halves
    part = half_rows // rows
    split = own.reshape(halves, half_rows, -1)
    held = split[0]
    for h in range(1, halves):
        got = lax.ppermute(split[h], AXES, [(k, k + h * sections) for k in range(sections)])
        held = jnp.where(col // sections == h, got, held)
    mine = lax.all_to_all(held.reshape(rows, part, -1), "row", 0, 0, tiled=True)[0]
    gathered = lax.all_gather(mine, AXES, tiled=True)

    update = jnp.concatenate([lead[None], rest], axis=0)
    update = update - jnp.einsum(
        "kjwhrt,rhkts->jws",
        panels.reshape(sections, blocks, width_block, halves, rows, part),
        gathered.reshape(rows, halves, sections, part, -1),
        precision=lax.Precision.HIGH,
        preferred_element_type=jnp.float32,
    )
    first = jnp.where(device < sections, own, update[0])
    return jnp.concatenate([first[None], update[1:]], axis=0)


def solution(mesh):
    in_specs = (P(AXES, None), P(None, None, AXES, None), P())
    out_specs = P(None, AXES, None)
    return jax.shard_map(
        per_device, mesh=mesh, in_specs=in_specs, out_specs=out_specs, check_vma=False
    )
```

```python
import jax
import jax.numpy as jnp
from jax import lax
from jax.sharding import PartitionSpec as P

AXES = ("row", "col")
HI = lax.Precision.HIGHEST


def mm(a, b):
    return jnp.dot(a, b, precision=HI, preferred_element_type=jnp.float32)


def transpose_in(pieces, devices):
    local_count, blocks, _, width_block = pieces.shape
    arrived = lax.all_to_all(pieces, AXES, split_axis=2, concat_axis=0, tiled=True)
    return jnp.transpose(arrived.reshape(devices * local_count, blocks, width_block), (1, 2, 0))


def per_device(snapshots, panels, diag_inverse):
    local_count, order_size = snapshots.shape
    sections, blocks, width_block, _ = panels.shape
    devices = lax.axis_size(AXES)
    cols = lax.axis_size("col")
    pieces = snapshots.reshape(local_count, blocks, devices, width_block)
    lead = transpose_in(pieces[:, :1], devices)[0]
    rest = transpose_in(pieces[:, 1:], devices)
    device = lax.axis_index(AXES)
    row = lax.axis_index("row")
    col = lax.axis_index("col")
    inverse = lax.dynamic_index_in_dim(
        diag_inverse, jnp.minimum(device, sections - 1), 0, keepdims=False
    )
    low = jnp.stack([mm(inverse, panels[k, 0]) for k in range(sections - 1)])

    after = [[None] * 3 for _ in range(sections)]
    first_hop = [None] * sections
    own = jnp.zeros_like(lead)
    settled = mm(inverse, lead)
    for section in range(sections):
        chain = settled
        if section >= 1:
            chain = chain - mm(low[section - 1], first_hop[section - 1])
        for back in (2, 3):
            if section - back >= 0:
                chain = chain - mm(low[section - back], after[section - back][1])
        solved = chain
        here = device == section
        own = jnp.where(here, solved, own)
        buf = jnp.where(here, solved, jnp.zeros_like(solved))
        for level in range(3):
            step = 2**level
            pairs = [
                (section + q, section + q + step)
                for q in range(step)
                if section + q + step < sections
            ]
            if pairs:
                got = lax.ppermute(buf, AXES, pairs)
                if level == 0:
                    first_hop[section] = got
                buf = buf + got
            after[section][level] = buf
        if section - 3 >= 0:
            settled = settled - mm(low[section - 3], after[section - 3][2])

    rows = lax.axis_size("row")
    halves = cols // sections
    half_rows = width_block // halves
    part = half_rows // rows
    split = own.reshape(halves, half_rows, -1)
    held = split[0]
    for h in range(1, halves):
        got = lax.ppermute(split[h], AXES, [(k, k + h * sections) for k in range(sections)])
        held = jnp.where(col // sections == h, got, held)
    mine = lax.all_to_all(held.reshape(rows, part, -1), "row", 0, 0, tiled=True)[0]
    gathered = lax.all_gather(mine, AXES, tiled=True)

    update = jnp.concatenate([lead[None], rest], axis=0)
    flat = panels.reshape(sections, blocks, width_block, halves, rows, part)
    solved_rows = gathered.reshape(rows, halves, sections, part, -1)

    def parts(a):
        high = lax.reduce_precision(a, exponent_bits=8, mantissa_bits=7)
        return high.astype(jnp.bfloat16), (a - high).astype(jnp.bfloat16)

    flat_hi, flat_lo = parts(flat)
    rows_hi, rows_lo = parts(solved_rows)

    def term(a, b):
        return jnp.einsum("kjwhrt,rhkts->jws", a, b, preferred_element_type=jnp.float32)

    update = update - (term(flat_hi, rows_hi) + (term(flat_hi, rows_lo) + term(flat_lo, rows_hi)))
    first = jnp.where(device < sections, own, update[0])
    return jnp.concatenate([first[None], update[1:]], axis=0)


def solution(mesh):
    in_specs = (P(AXES, None), P(None, None, AXES, None), P())
    out_specs = P(None, AXES, None)
    return jax.shard_map(
        per_device, mesh=mesh, in_specs=in_specs, out_specs=out_specs, check_vma=False
    )
```
